128 devices in a mesh: dp: 32 (over x_lo, z, y), mp: 4 (over x_hi, core).
Axes of the slice: x: 4 (x_hi: 2, x_lo: 2; x = x_hi * 2 + x_lo), y: 4, z: 4, core: 2. Of those that a mesh axis runs over, the one named last changes fastest.
Arguments:
- samples: bfloat16 [24576, 8192], P('dp', 'mp'), may hold values from -6 to 6
- gain: float32 [8192], P('mp'), may hold values from 0.1 to 1.9
- left_blocks: bfloat16 [64, 128, 128], P('mp'), may hold values from -0.5 to 0.5
- gate_blocks: bfloat16 [64, 128, 128], P('mp'), may hold values from -0.5 to 0.5
- right_blocks: bfloat16 [64, 128, 128], P('mp'), may hold values from -0.5 to 0.5
- cotangent: bfloat16 [24576, 8192], P('dp', 'mp'), may hold values from -6 to 6
Outputs:
- grad_input: bfloat16 [24576, 8192], P('dp', 'mp')
- grad_left: float32 [64, 128, 128], P('mp')
- grad_gate: float32 [64, 128, 128], P('mp')
- grad_right: float32 [64, 128, 128], P('mp')
The draws below stay inside these ranges and needn't reach their ends.
All inputs are finite; a program needn't handle non-finite values.
Results may differ from the reference program's by a relative error of at most 0.007.
Values may be sent and summed in bfloat16 or wider, within the bound.
No kernel may reach another device: no remote copies, remote signals or barrier semaphores. Data moves between devices by JAX's collectives and lax.ppermute only.
A program may use at most 128 MiB of HBM per device.

```python
import jax
import jax.numpy as jnp
from jax import lax

W = 8192
BLOCK = 128
NBLK = 64
ROWS_DEV = 768
TOKENS = 24576


def block_levels(own_key, shape, split, least, largest):
    level, own = 1.0, jax.random.fold_in(own_key, 6)
    for position, shards_of in split:
        heights = jnp.exp(jax.random.uniform(jax.random.fold_in(own, position), (shards_of,), jnp.float32, least / len(split), largest / len(split)))
        level = level * jnp.repeat(heights, shape[position] // shards_of).reshape([-1 if axis == position else 1 for axis in range(len(shape))])
    return level


def gaussian(rng, extent, spread, reach, pieces=(), held_as=jnp.bfloat16):
    loudness = block_levels(rng, extent, pieces, -0.22, 0.18) if pieces else 1.0
    drawn = jax.random.normal(rng, extent, jnp.float32) * spread * loudness
    return jnp.minimum(jnp.maximum(drawn, -reach), reach).astype(held_as)


def setup_inputs(seed: int = 0) -> dict:
    seeds = jax.random.split(jax.random.key(seed), 7)
    samples = gaussian(seeds[0], (TOKENS, W), 1.0, 6.0, ((0, 32), (1, 4)))
    gain = jnp.clip(1.0 + 0.18 * jax.random.normal(seeds[1], (W,), jnp.float32), 0.1, 1.9)
    left_blocks = gaussian(seeds[2], (NBLK, BLOCK, BLOCK), BLOCK ** -0.5, 0.5, ((0, 4),))
    gate_blocks = gaussian(seeds[3], (NBLK, BLOCK, BLOCK), BLOCK ** -0.5, 0.5, ((0, 4),))
    right_blocks = gaussian(seeds[4], (NBLK, BLOCK, BLOCK), BLOCK ** -0.5, 0.5, ((0, 4),))
    cotangent = gaussian(seeds[5], (TOKENS, W), 1.0, 6.0, ((0, 32), (1, 4)))
    return {"samples": samples, "gain": gain, "left_blocks": left_blocks, "gate_blocks": gate_blocks, "right_blocks": right_blocks, "cotangent": cotangent}


def frame_block(xblk, dyblk, gain, left_blocks, gate_blocks, right_blocks):
    count = xblk.shape[0]
    xf = xblk.astype(jnp.float32)
    rstd = lax.rsqrt(lax.optimization_barrier(jnp.sum(xf * xf, axis=1, keepdims=True)) / W + 1e-05)
    xn = (xf * rstd * gain).astype(jnp.bfloat16).reshape(count, NBLK, BLOCK).astype(jnp.float32)
    lf = left_blocks.astype(jnp.float32)
    gf = gate_blocks.astype(jnp.float32)
    rf = right_blocks.astype(jnp.float32)
    a = jnp.einsum('tic,icj->tij', xn, lf)
    g = jnp.einsum('tic,icj->tij', xn, gf)
    sg = jax.nn.silu(g)
    h = (a * sg).astype(jnp.bfloat16)
    p = h.reshape(count, NBLK, NBLK, 2).transpose(0, 2, 1, 3).reshape(count, NBLK, BLOCK).astype(jnp.float32)
    dyr = dyblk.reshape(count, NBLK, BLOCK).astype(jnp.float32)
    d_right = jnp.einsum('tkc,tkm->kcm', p, dyr)
    dp = jnp.einsum('tkm,kcm->tkc', dyr, rf).astype(jnp.bfloat16)
    dh = dp.reshape(count, NBLK, NBLK, 2).transpose(0, 2, 1, 3).reshape(count, NBLK, BLOCK).astype(jnp.float32)
    sig = jax.nn.sigmoid(g)
    da = (dh * sg).astype(jnp.bfloat16).astype(jnp.float32)
    dg = (dh * a * sig * (1.0 + g * (1.0 - sig))).astype(jnp.bfloat16).astype(jnp.float32)
    d_left = jnp.einsum('tic,tij->icj', xn, da)
    d_gate = jnp.einsum('tic,tij->icj', xn, dg)
    dxn = jnp.einsum('tij,icj->tic', da, lf) + jnp.einsum('tij,icj->tic', dg, gf)
    q = dxn.reshape(count, W) * gain
    mu = lax.optimization_barrier(jnp.sum(q * xf, axis=1, keepdims=True)) / W
    dx = (dyblk.astype(jnp.float32) + rstd * (q - xf * rstd * rstd * mu)).astype(jnp.bfloat16)
    return (dx, d_left, d_gate, d_right)

def reference(samples, gain, left_blocks, gate_blocks, right_blocks, cotangent):
    nsteps = TOKENS // ROWS_DEV
    xs = samples.reshape(nsteps, ROWS_DEV, W)
    dys = cotangent.reshape(nsteps, ROWS_DEV, W)
    zero = jnp.zeros((NBLK, BLOCK, BLOCK), jnp.float32)

    def step(carry, inputs):
        dx, d_left, d_gate, d_right = frame_block(inputs[0], inputs[1], gain, left_blocks, gate_blocks, right_blocks)
        return ((carry[0] + d_left, carry[1] + d_gate, carry[2] + d_right), dx)
    sums, dxs = lax.scan(step, (zero, zero, zero), (xs, dys))
    return (dxs.reshape(TOKENS, W), sums[0], sums[1], sums[2])
```

```python
import jax
import jax.numpy as jnp
from jax import lax
from jax.sharding import PartitionSpec as P

W = 8192
BLOCK = 128
NBLK = 64


def body(samples, gain, left_blocks, gate_blocks, right_blocks, cotangent):
    rows, width_local = samples.shape
    nlocal = left_blocks.shape[0]
    xf = samples.astype(jnp.float32)
    squares = lax.psum(jnp.sum(xf * xf, axis=1), "mp")
    rstd = lax.rsqrt(squares / W + 1e-05)[:, None]
    xn = (xf * rstd * gain).astype(jnp.bfloat16).reshape(rows, nlocal, BLOCK)
    act_a = jnp.einsum("tic,icj->tij", xn, left_blocks, preferred_element_type=jnp.float32)
    act_g = jnp.einsum("tic,icj->tij", xn, gate_blocks, preferred_element_type=jnp.float32)
    silu_g = jax.nn.silu(act_g)
    gated = (act_a * silu_g).astype(jnp.bfloat16)
    outgoing = (
        gated.reshape(rows, nlocal, NBLK, 2).transpose(0, 2, 1, 3).reshape(rows, NBLK, 2 * nlocal)
    )
    cot_blocks = cotangent.reshape(rows, nlocal, BLOCK)
    grad_perm = jnp.einsum(
        "tkm,kcm->tkc", cot_blocks, right_blocks, preferred_element_type=jnp.float32
    ).astype(jnp.bfloat16)
    permuted = lax.all_to_all(outgoing, "mp", split_axis=1, concat_axis=2, tiled=True)
    right_local = jnp.einsum(
        "tkc,tkm->kcm", permuted, cot_blocks, preferred_element_type=jnp.float32
    )
    returned = lax.all_to_all(grad_perm, "mp", split_axis=2, concat_axis=1, tiled=True)
    grad_gated = (
        returned.reshape(rows, NBLK, nlocal, 2)
        .transpose(0, 2, 1, 3)
        .reshape(rows, nlocal, BLOCK)
        .astype(jnp.float32)
    )
    sigma = jax.nn.sigmoid(act_g)
    grad_a = (grad_gated * silu_g).astype(jnp.bfloat16)
    grad_g = (grad_gated * act_a * sigma * (1.0 + act_g * (1.0 - sigma))).astype(jnp.bfloat16)
    left_local = jnp.einsum("tic,tij->icj", xn, grad_a, preferred_element_type=jnp.float32)
    gate_local = jnp.einsum("tic,tij->icj", xn, grad_g, preferred_element_type=jnp.float32)
    grad_norm = jnp.einsum("tij,icj->tic", grad_a, left_blocks, preferred_element_type=jnp.float32)
    grad_norm = grad_norm + jnp.einsum(
        "tij,icj->tic", grad_g, gate_blocks, preferred_element_type=jnp.float32
    )
    scaled = grad_norm.reshape(rows, width_local) * gain
    inner = lax.psum(jnp.sum(scaled * xf, axis=1), "mp")
    mean_inner = (inner / W)[:, None]
    grad_input = (
        cotangent.astype(jnp.float32) + rstd * (scaled - xf * rstd * rstd * mean_inner)
    ).astype(jnp.bfloat16)
    left_total, gate_total, right_total = dp_all_reduce((left_local, gate_local, right_local))
    return (grad_input, left_total, gate_total, right_total)


def dp_all_reduce(parts):
    ndp = lax.axis_size("dp")
    shapes = [p.shape for p in parts]
    flat = jnp.concatenate([p.reshape(-1) for p in parts]).reshape(ndp, -1)
    mine = jnp.sum(lax.all_to_all(flat, "dp", 0, 0, tiled=True), axis=0)
    copies = jnp.broadcast_to(mine[None], (ndp,) + mine.shape)
    whole = lax.all_to_all(copies, "dp", 0, 0, tiled=True).reshape(-1)
    out, at = [], 0
    for shape in shapes:
        size = shape[0] * shape[1] * shape[2]
        out.append(whole[at:at + size].reshape(shape))
        at += size
    return tuple(out)


def solution(mesh):
    placed = (
        P("dp", "mp"),
        P("mp"),
        P("mp", None, None),
        P("mp", None, None),
        P("mp", None, None),
        P("dp", "mp"),
    )
    return jax.shard_map(
        body,
        mesh=mesh,
        in_specs=placed,
        out_specs=(P("dp", "mp"), P("mp", None, None), P("mp", None, None), P("mp", None, None)),
        check_vma=False,
    )
```

```python
import jax
import jax.numpy as jnp
from jax import lax
from jax.sharding import PartitionSpec as P

W = 8192
BLOCK = 128
NBLK = 64


def dp_all_reduce(parts):
    ndp = lax.axis_size("dp")
    shapes = [p.shape for p in parts]
    flat = jnp.concatenate([p.reshape(-1) for p in parts]).reshape(ndp, -1)
    mine = jnp.sum(lax.all_to_all(flat, "dp", 0, 0, tiled=True), axis=0)
    copies = jnp.broadcast_to(mine[None], (ndp,) + mine.shape)
    whole = lax.all_to_all(copies, "dp", 0, 0, tiled=True).reshape(-1)
    out, at = [], 0
    for shape in shapes:
        size = shape[0] * shape[1] * shape[2]
        out.append(whole[at:at + size].reshape(shape))
        at += size
    return tuple(out)


def body(samples, gain, left_blocks, gate_blocks, right_blocks, cotangent):
    rows, width_local = samples.shape
    nlocal = left_blocks.shape[0]
    xf = samples.astype(jnp.float32)
    cot_blocks = cotangent.reshape(rows, nlocal, BLOCK)
    grad_perm = jnp.einsum(
        "tkm,kcm->tkc", cot_blocks, right_blocks, preferred_element_type=jnp.float32
    ).astype(jnp.bfloat16)
    squares = lax.psum(jnp.sum(xf * xf, axis=1), "mp")
    grad_perm, squares = lax.optimization_barrier((grad_perm, squares))
    rstd = lax.rsqrt(squares / W + 1e-05)[:, None]
    xn = (xf * rstd * gain).astype(jnp.bfloat16).reshape(rows, nlocal, BLOCK)
    act_a = jnp.einsum("tic,icj->tij", xn, left_blocks, preferred_element_type=jnp.float32)
    act_g = jnp.einsum("tic,icj->tij", xn, gate_blocks, preferred_element_type=jnp.float32)
    gated = (act_a * jax.nn.silu(act_g)).astype(jnp.bfloat16)
    outgoing = (
        gated.reshape(rows, nlocal, NBLK, 2).transpose(0, 2, 1, 3).reshape(rows, NBLK, 2 * nlocal)
    )
    returned = lax.all_to_all(grad_perm, "mp", split_axis=2, concat_axis=1, tiled=True)
    outgoing, xn_b = lax.optimization_barrier((outgoing, xn))
    permuted = lax.all_to_all(outgoing, "mp", split_axis=1, concat_axis=2, tiled=True)
    right_local = jnp.einsum(
        "tkc,tkm->kcm", permuted, cot_blocks, preferred_element_type=jnp.float32
    )
    (right_total,) = dp_all_reduce((right_local,))
    act_a = jnp.einsum("tic,icj->tij", xn_b, left_blocks, preferred_element_type=jnp.float32)
    act_g = jnp.einsum("tic,icj->tij", xn_b, gate_blocks, preferred_element_type=jnp.float32)
    silu_g = jax.nn.silu(act_g)
    grad_gated = (
        returned.reshape(rows, NBLK, nlocal, 2)
        .transpose(0, 2, 1, 3)
        .reshape(rows, nlocal, BLOCK)
        .astype(jnp.float32)
    )
    sigma = jax.nn.sigmoid(act_g)
    grad_a = (grad_gated * silu_g).astype(jnp.bfloat16)
    grad_g = (grad_gated * act_a * sigma * (1.0 + act_g * (1.0 - sigma))).astype(jnp.bfloat16)
    left_local = jnp.einsum("tic,tij->icj", xn_b, grad_a, preferred_element_type=jnp.float32)
    gate_local = jnp.einsum("tic,tij->icj", xn_b, grad_g, preferred_element_type=jnp.float32)
    grad_norm = jnp.einsum("tij,icj->tic", grad_a, left_blocks, preferred_element_type=jnp.float32)
    grad_norm = grad_norm + jnp.einsum(
        "tij,icj->tic", grad_g, gate_blocks, preferred_element_type=jnp.float32
    )
    scaled = grad_norm.reshape(rows, width_local) * gain
    inner = lax.psum(jnp.sum(scaled * xf, axis=1), "mp")
    mean_inner = (inner / W)[:, None]
    grad_input = (
        cotangent.astype(jnp.float32) + rstd * (scaled - xf * rstd * rstd * mean_inner)
    ).astype(jnp.bfloat16)
    left_total, gate_total = dp_all_reduce((left_local, gate_local))
    return (grad_input, left_total, gate_total, right_total)


def solution(mesh):
    placed = (
        P("dp", "mp"),
        P("mp"),
        P("mp", None, None),
        P("mp", None, None),
        P("mp", None, None),
        P("dp", "mp"),
    )
    return jax.shard_map(
        body,
        mesh=mesh,
        in_specs=placed,
        out_specs=(P("dp", "mp"), P("mp", None, None), P("mp", None, None), P("mp", None, None)),
        check_vma=False,
    )
```

```python
import jax
import jax.numpy as jnp
from jax import lax
from jax.sharding import PartitionSpec as P

W = 8192
BLOCK = 128
NBLK = 64


def dp_reduce_scatter(parts):
    ndp = lax.axis_size("dp")
    flat = jnp.concatenate([p.reshape(-1) for p in parts]).reshape(ndp, 16, -1)
    got = lax.all_to_all(flat.astype(jnp.bfloat16), "dp", 0, 0, tiled=True)
    return jnp.sum(got.astype(jnp.float32), axis=0)


def dp_all_gather(mine, shapes):
    ndp = lax.axis_size("dp")
    copies = jnp.broadcast_to(mine.astype(jnp.bfloat16)[None], (ndp,) + mine.shape)
    whole = lax.all_to_all(copies, "dp", 0, 0, tiled=True).reshape(-1).astype(jnp.float32)
    out, at = [], 0
    for shape in shapes:
        size = shape[0] * shape[1] * shape[2]
        out.append(whole[at:at + size].reshape(shape))
        at += size
    return tuple(out)


def body(samples, gain, left_blocks, gate_blocks, right_blocks, cotangent):
    rows, width_local = samples.shape
    nlocal = left_blocks.shape[0]
    xf = samples.astype(jnp.float32)
    cot_blocks = cotangent.reshape(rows, nlocal, BLOCK)
    grad_perm = jnp.einsum(
        "tkm,kcm->tkc", cot_blocks, right_blocks, preferred_element_type=jnp.float32
    ).astype(jnp.bfloat16)
    squares = lax.psum(jnp.sum(xf * xf, axis=1), "mp")
    grad_perm, squares = lax.optimization_barrier((grad_perm, squares))
    rstd = lax.rsqrt(squares / W + 1e-05)[:, None]
    xn = (xf * rstd * gain).astype(jnp.bfloat16).reshape(rows, nlocal, BLOCK)
    act_a = jnp.einsum("tic,icj->tij", xn, left_blocks, preferred_element_type=jnp.float32)
    act_g = jnp.einsum("tic,icj->tij", xn, gate_blocks, preferred_element_type=jnp.float32)
    gated = (act_a * jax.nn.silu(act_g)).astype(jnp.bfloat16)
    outgoing = (
        gated.reshape(rows, nlocal, NBLK, 2).transpose(0, 2, 1, 3).reshape(rows, NBLK, 2 * nlocal)
    )
    returned = lax.all_to_all(grad_perm, "mp", split_axis=2, concat_axis=1, tiled=True)
    outgoing, xn_b = lax.optimization_barrier((outgoing, xn))
    permuted = lax.all_to_all(outgoing, "mp", split_axis=1, concat_axis=2, tiled=True)
    right_local = jnp.einsum(
        "tkc,tkm->kcm", permuted, cot_blocks, preferred_element_type=jnp.float32
    )
    act_a = jnp.einsum("tic,icj->tij", xn_b, left_blocks, preferred_element_type=jnp.float32)
    act_g = jnp.einsum("tic,icj->tij", xn_b, gate_blocks, preferred_element_type=jnp.float32)
    silu_g = jax.nn.silu(act_g)
    grad_gated = (
        returned.reshape(rows, NBLK, nlocal, 2)
        .transpose(0, 2, 1, 3)
        .reshape(rows, nlocal, BLOCK)
        .astype(jnp.float32)
    )
    sigma = jax.nn.sigmoid(act_g)
    grad_a = (grad_gated * silu_g).astype(jnp.bfloat16)
    grad_g = (grad_gated * act_a * sigma * (1.0 + act_g * (1.0 - sigma))).astype(jnp.bfloat16)
    left_local = jnp.einsum("tic,tij->icj", xn_b, grad_a, preferred_element_type=jnp.float32)
    gate_local = jnp.einsum("tic,tij->icj", xn_b, grad_g, preferred_element_type=jnp.float32)
    grad_norm = jnp.einsum("tij,icj->tic", grad_a, left_blocks, preferred_element_type=jnp.float32)
    grad_norm = grad_norm + jnp.einsum(
        "tij,icj->tic", grad_g, gate_blocks, preferred_element_type=jnp.float32
    )
    partials = (left_local, gate_local, right_local)
    mine = dp_reduce_scatter(partials)
    scaled = grad_norm.reshape(rows, width_local) * gain
    mine, scaled = lax.optimization_barrier((mine, scaled))
    inner = lax.psum(jnp.sum(scaled * xf, axis=1), "mp")
    mean_inner = (inner / W)[:, None]
    grad_input = (
        cotangent.astype(jnp.float32) + rstd * (scaled - xf * rstd * rstd * mean_inner)
    ).astype(jnp.bfloat16)
    left_total, gate_total, right_total = dp_all_gather(mine, [p.shape for p in partials])
    return (grad_input, left_total, gate_total, right_total)


def solution(mesh):
    placed = (
        P("dp", "mp"),
        P("mp"),
        P("mp", None, None),
        P("mp", None, None),
        P("mp", None, None),
        P("dp", "mp"),
    )
    return jax.shard_map(
        body,
        mesh=mesh,
        in_specs=placed,
        out_specs=(P("dp", "mp"), P("mp", None, None), P("mp", None, None), P("mp", None, None)),
        check_vma=False,
    )
```

```python
import jax
import jax.numpy as jnp
from jax import lax
from jax.sharding import PartitionSpec as P

W = 8192
BLOCK = 128
NBLK = 64


def dp_reduce_scatter(parts):
    ndp = lax.axis_size("dp")
    flat = jnp.concatenate([p.reshape(-1, BLOCK) for p in parts]).reshape(ndp, -1, BLOCK)
    got = lax.all_to_all(flat, "dp", 0, 0, tiled=True)
    return jnp.sum(got, axis=0)


def dp_all_gather(mine, shapes):
    ndp = lax.axis_size("dp")
    copies = jnp.broadcast_to(mine.astype(jnp.bfloat16)[None], (ndp,) + mine.shape)
    whole = lax.all_to_all(copies, "dp", 0, 0, tiled=True).reshape(-1, BLOCK, BLOCK)
    out, at = [], 0
    for shape in shapes:
        out.append(whole[at:at + shape[0]].astype(jnp.float32))
        at += shape[0]
    return tuple(out)


def body(samples, gain, left_blocks, gate_blocks, right_blocks, cotangent):
    rows, width_local = samples.shape
    nlocal = left_blocks.shape[0]
    xf = samples.astype(jnp.float32)
    cot_blocks = cotangent.reshape(rows, nlocal, BLOCK)
    grad_perm = jnp.einsum(
        "tkm,kcm->tkc", cot_blocks, right_blocks, preferred_element_type=jnp.float32
    ).astype(jnp.bfloat16)
    squares = lax.psum(jnp.sum(xf * xf, axis=1), "mp")
    grad_perm, squares = lax.optimization_barrier((grad_perm, squares))
    rstd = lax.rsqrt(squares / W + 1e-05)[:, None]
    xn = (xf * rstd * gain).astype(jnp.bfloat16).reshape(rows, nlocal, BLOCK)
    act_a = jnp.einsum("tic,icj->tij", xn, left_blocks, preferred_element_type=jnp.float32)
    act_g = jnp.einsum("tic,icj->tij", xn, gate_blocks, preferred_element_type=jnp.float32)
    gated = (act_a * jax.nn.silu(act_g)).astype(jnp.bfloat16)
    outgoing = (
        gated.reshape(rows, nlocal, NBLK, 2).transpose(0, 2, 1, 3).reshape(rows, NBLK, 2 * nlocal)
    )
    returned = lax.all_to_all(grad_perm, "mp", split_axis=2, concat_axis=1, tiled=True)
    outgoing, xn_b = lax.optimization_barrier((outgoing, xn))
    permuted = lax.all_to_all(outgoing, "mp", split_axis=1, concat_axis=2, tiled=True)
    right_local = jnp.einsum(
        "tkc,tkm->kcm", permuted, cot_blocks, preferred_element_type=jnp.float32
    )
    act_a = jnp.einsum("tic,icj->tij", xn_b, left_blocks, preferred_element_type=jnp.float32)
    act_g = jnp.einsum("tic,icj->tij", xn_b, gate_blocks, preferred_element_type=jnp.float32)
    silu_g = jax.nn.silu(act_g)
    grad_gated = (
        returned.reshape(rows, NBLK, nlocal, 2)
        .transpose(0, 2, 1, 3)
        .reshape(rows, nlocal, BLOCK)
        .astype(jnp.float32)
    )
    sigma = jax.nn.sigmoid(act_g)
    grad_a = (grad_gated * silu_g).astype(jnp.bfloat16)
    grad_g = (grad_gated * act_a * sigma * (1.0 + act_g * (1.0 - sigma))).astype(jnp.bfloat16)
    left_local = jnp.einsum("tic,tij->icj", xn_b, grad_a, preferred_element_type=jnp.float32)
    gate_local = jnp.einsum("tic,tij->icj", xn_b, grad_g, preferred_element_type=jnp.float32)
    grad_norm = jnp.einsum("tij,icj->tic", grad_a, left_blocks, preferred_element_type=jnp.float32)
    grad_norm = grad_norm + jnp.einsum(
        "tij,icj->tic", grad_g, gate_blocks, preferred_element_type=jnp.float32
    )
    partials = (left_local, gate_local, right_local)
    mine = dp_reduce_scatter(partials)
    scaled = grad_norm.reshape(rows, width_local) * gain
    mine, scaled = lax.optimization_barrier((mine, scaled))
    inner = lax.psum(jnp.sum(scaled * xf, axis=1), "mp")
    mean_inner = (inner / W)[:, None]
    grad_input = (
        cotangent.astype(jnp.float32) + rstd * (scaled - xf * rstd * rstd * mean_inner)
    ).astype(jnp.bfloat16)
    left_total, gate_total, right_total = dp_all_gather(mine, [p.shape for p in partials])
    return (grad_input, left_total, gate_total, right_total)


def solution(mesh):
    placed = (
        P("dp", "mp"),
        P("mp"),
        P("mp", None, None),
        P("mp", None, None),
        P("mp", None, None),
        P("dp", "mp"),
    )
    return jax.shard_map(
        body,
        mesh=mesh,
        in_specs=placed,
        out_specs=(P("dp", "mp"), P("mp", None, None), P("mp", None, None), P("mp", None, None)),
        check_vma=False,
    )
```

```python
import jax
import jax.numpy as jnp
from jax import lax
from jax.sharding import PartitionSpec as P

W = 8192
BLOCK = 128
NBLK = 64


def dp_reduce_scatter(parts):
    ndp = lax.axis_size("dp")
    flat = jnp.concatenate([p.reshape(-1, BLOCK) for p in parts]).reshape(ndp, -1, BLOCK)
    got = lax.all_to_all(flat, "dp", 0, 0, tiled=True)
    return jnp.sum(got, axis=0)


def dp_all_gather(mine, shapes):
    ndp = lax.axis_size("dp")
    copies = jnp.broadcast_to(mine.astype(jnp.bfloat16)[None], (ndp,) + mine.shape)
    whole = lax.all_to_all(copies, "dp", 0, 0, tiled=True).reshape(-1, BLOCK, BLOCK)
    out, at = [], 0
    for shape in shapes:
        out.append(whole[at:at + shape[0]].astype(jnp.float32))
        at += shape[0]
    return tuple(out)


def pair_major(blocks):
    n, c, _ = blocks.shape
    return blocks.reshape(n, c, NBLK, 2).transpose(0, 1, 3, 2).reshape(n, c, 2 * NBLK)


def pair_minor(blocks):
    n, c, _ = blocks.shape
    return blocks.reshape(n, c, 2, NBLK).transpose(0, 1, 3, 2).reshape(n, c, 2 * NBLK)


def body(samples, gain, left_blocks, gate_blocks, right_blocks, cotangent):
    rows, width_local = samples.shape
    nlocal = left_blocks.shape[0]
    xf = samples.astype(jnp.float32)
    cot_blocks = cotangent.reshape(rows, nlocal, BLOCK)
    grad_perm = jnp.einsum(
        "tkm,kcm->tkc", cot_blocks, right_blocks, preferred_element_type=jnp.float32
    ).astype(jnp.bfloat16)
    squares = lax.psum(jnp.sum(xf * xf, axis=1), "mp")
    grad_perm, squares = lax.optimization_barrier((grad_perm, squares))
    rstd = lax.rsqrt(squares / W + 1e-05)[:, None]
    xn = (xf * rstd * gain).astype(jnp.bfloat16).reshape(rows, nlocal, BLOCK)
    left_p = pair_major(left_blocks)
    gate_p = pair_major(gate_blocks)
    act_a = jnp.einsum("tic,icj->tij", xn, left_p, preferred_element_type=jnp.float32)
    act_g = jnp.einsum("tic,icj->tij", xn, gate_p, preferred_element_type=jnp.float32)
    gated = (act_a * jax.nn.silu(act_g)).astype(jnp.bfloat16)
    outgoing = (
        gated.reshape(rows, nlocal, 2, NBLK).transpose(0, 3, 1, 2).reshape(rows, NBLK, 2 * nlocal)
    )
    returned = lax.all_to_all(grad_perm, "mp", split_axis=2, concat_axis=1, tiled=True)
    outgoing, xn_b = lax.optimization_barrier((outgoing, xn))
    permuted = lax.all_to_all(outgoing, "mp", split_axis=1, concat_axis=2, tiled=True)
    right_local = jnp.einsum(
        "tkc,tkm->kcm", permuted, cot_blocks, preferred_element_type=jnp.float32
    )
    act_a = jnp.einsum("tic,icj->tij", xn_b, left_p, preferred_element_type=jnp.float32)
    act_g = jnp.einsum("tic,icj->tij", xn_b, gate_p, preferred_element_type=jnp.float32)
    silu_g = jax.nn.silu(act_g)
    grad_gated = (
        returned.reshape(rows, NBLK, nlocal, 2)
        .transpose(0, 2, 3, 1)
        .reshape(rows, nlocal, BLOCK)
        .astype(jnp.float32)
    )
    sigma = jax.nn.sigmoid(act_g)
    grad_a = (grad_gated * silu_g).astype(jnp.bfloat16)
    grad_g = (grad_gated * act_a * sigma * (1.0 + act_g * (1.0 - sigma))).astype(jnp.bfloat16)
    left_local = pair_minor(jnp.einsum("tic,tij->icj", xn_b, grad_a, preferred_element_type=jnp.float32))
    gate_local = pair_minor(jnp.einsum("tic,tij->icj", xn_b, grad_g, preferred_element_type=jnp.float32))
    grad_norm = jnp.einsum("tij,icj->tic", grad_a, left_p, preferred_element_type=jnp.float32)
    grad_norm = grad_norm + jnp.einsum(
        "tij,icj->tic", grad_g, gate_p, preferred_element_type=jnp.float32
    )
    partials = (left_local, gate_local, right_local)
    mine = dp_reduce_scatter(partials)
    scaled = grad_norm.reshape(rows, width_local) * gain
    mine, scaled = lax.optimization_barrier((mine, scaled))
    inner = lax.psum(jnp.sum(scaled * xf, axis=1), "mp")
    mean_inner = (inner / W)[:, None]
    grad_input = (
        cotangent.astype(jnp.float32) + rstd * (scaled - xf * rstd * rstd * mean_inner)
    ).astype(jnp.bfloat16)
    left_total, gate_total, right_total = dp_all_gather(mine, [p.shape for p in partials])
    return (grad_input, left_total, gate_total, right_total)


def solution(mesh):
    placed = (
        P("dp", "mp"),
        P("mp"),
        P("mp", None, None),
        P("mp", None, None),
        P("mp", None, None),
        P("dp", "mp"),
    )
    return jax.shard_map(
        body,
        mesh=mesh,
        in_specs=placed,
        out_specs=(P("dp", "mp"), P("mp", None, None), P("mp", None, None), P("mp", None, None)),
        check_vma=False,
    )
```

```python
import jax
import jax.numpy as jnp
from jax import lax
from jax.sharding import PartitionSpec as P

W = 8192
BLOCK = 128
NBLK = 64


def dp_reduce_scatter(parts):
    ndp = lax.axis_size("dp")
    flat = jnp.concatenate([p.reshape(-1, BLOCK) for p in parts]).reshape(ndp, -1, BLOCK)
    got = lax.all_to_all(flat, "dp", 0, 0, tiled=True)
    return jnp.sum(got, axis=0)


def dp_all_gather(mine, shapes):
    ndp = lax.axis_size("dp")
    copies = jnp.broadcast_to(mine.astype(jnp.bfloat16)[None], (ndp,) + mine.shape)
    whole = lax.all_to_all(copies, "dp", 0, 0, tiled=True).reshape(-1, BLOCK, BLOCK)
    out, at = [], 0
    for shape in shapes:
        out.append(whole[at:at + shape[0]].astype(jnp.float32))
        at += shape[0]
    return tuple(out)


def pair_major(blocks):
    n, c, _ = blocks.shape
    return blocks.reshape(n, c, NBLK, 2).transpose(0, 1, 3, 2).reshape(n, c, 2 * NBLK)


def pair_minor(blocks):
    n, c, _ = blocks.shape
    return blocks.reshape(n, c, 2, NBLK).transpose(0, 1, 3, 2).reshape(n, c, 2 * NBLK)


def body(samples, gain, left_blocks, gate_blocks, right_blocks, cotangent):
    rows, width_local = samples.shape
    nlocal = left_blocks.shape[0]
    xf = samples.astype(jnp.float32)
    cot_blocks = cotangent.reshape(rows, nlocal, BLOCK)
    grad_perm = jnp.einsum(
        "tkm,kcm->tkc", cot_blocks, right_blocks, preferred_element_type=jnp.float32
    ).astype(jnp.bfloat16)
    squares = lax.psum(jnp.sum(xf * xf, axis=1), "mp")
    grad_perm, squares = lax.optimization_barrier((grad_perm, squares))
    rstd = lax.rsqrt(squares / W + 1e-05)[:, None]
    xn = (xf * rstd * gain).astype(jnp.bfloat16).reshape(rows, nlocal, BLOCK)
    left_p = pair_major(left_blocks)
    gate_p = pair_major(gate_blocks)
    act_a = jnp.einsum("tic,icj->tij", xn, left_p, preferred_element_type=jnp.float32)
    act_g = jnp.einsum("tic,icj->tij", xn, gate_p, preferred_element_type=jnp.float32)
    gated = (act_a * jax.nn.silu(act_g)).astype(jnp.bfloat16)
    outgoing = (
        gated.reshape(rows, nlocal, 2, NBLK).transpose(0, 3, 1, 2).reshape(rows, NBLK, 2 * nlocal)
    )
    returned = lax.all_to_all(grad_perm, "mp", split_axis=2, concat_axis=1, tiled=True)
    outgoing, xn_b = lax.optimization_barrier((outgoing, xn))
    permuted = lax.all_to_all(outgoing, "mp", split_axis=1, concat_axis=2, tiled=True)
    act_a = jnp.einsum("tic,icj->tij", xn_b, left_p, preferred_element_type=jnp.float32)
    act_g = jnp.einsum("tic,icj->tij", xn_b, gate_p, preferred_element_type=jnp.float32)
    silu_g = jax.nn.silu(act_g)
    grad_gated = (
        returned.reshape(rows, NBLK, nlocal, 2)
        .transpose(0, 2, 3, 1)
        .reshape(rows, nlocal, BLOCK)
        .astype(jnp.float32)
    )
    sigma = jax.nn.sigmoid(act_g)
    grad_a = (grad_gated * silu_g).astype(jnp.bfloat16)
    grad_g = (grad_gated * act_a * sigma * (1.0 + act_g * (1.0 - sigma))).astype(jnp.bfloat16)
    left_local = pair_minor(jnp.einsum("tic,tij->icj", xn_b, grad_a, preferred_element_type=jnp.float32))
    gate_local = pair_minor(jnp.einsum("tic,tij->icj", xn_b, grad_g, preferred_element_type=jnp.float32))
    grad_norm = jnp.einsum("tij,icj->tic", grad_a, left_p, preferred_element_type=jnp.float32)
    grad_norm = grad_norm + jnp.einsum(
        "tij,icj->tic", grad_g, gate_p, preferred_element_type=jnp.float32
    )
    permuted, left_local, gate_local, grad_norm = lax.optimization_barrier(
        (permuted, left_local, gate_local, grad_norm)
    )
    right_local = jnp.einsum(
        "tkc,tkm->kcm", permuted, cot_blocks, preferred_element_type=jnp.float32
    )
    partials = (left_local, gate_local, right_local)
    mine = dp_reduce_scatter(partials)
    scaled = grad_norm.reshape(rows, width_local) * gain
    inner = lax.psum(jnp.sum(scaled * xf, axis=1), "mp")
    mean_inner = (inner / W)[:, None]
    grad_input = (
        cotangent.astype(jnp.float32) + rstd * (scaled - xf * rstd * rstd * mean_inner)
    ).astype(jnp.bfloat16)
    mine, grad_input = lax.optimization_barrier((mine, grad_input))
    left_total, gate_total, right_total = dp_all_gather(mine, [p.shape for p in partials])
    return (grad_input, left_total, gate_total, right_total)


def solution(mesh):
    placed = (
        P("dp", "mp"),
        P("mp"),
        P("mp", None, None),
        P("mp", None, None),
        P("mp", None, None),
        P("dp", "mp"),
    )
    return jax.shard_map(
        body,
        mesh=mesh,
        in_specs=placed,
        out_specs=(P("dp", "mp"), P("mp", None, None), P("mp", None, None), P("mp", None, None)),
        check_vma=False,
    )
```

```python
import jax
import jax.numpy as jnp
from jax import lax
from jax.sharding import PartitionSpec as P

W = 8192
BLOCK = 128
NBLK = 64


def dp_reduce_scatter(parts):
    ndp = lax.axis_size("dp")
    flat = jnp.concatenate([p.reshape(-1, BLOCK) for p in parts]).reshape(ndp, -1, BLOCK)
    got = lax.all_to_all(flat, "dp", 0, 0, tiled=True)
    return jnp.sum(got, axis=0)


def dp_all_gather(mine, shapes):
    ndp = lax.axis_size("dp")
    copies = jnp.broadcast_to(mine.astype(jnp.bfloat16)[None], (ndp,) + mine.shape)
    whole = lax.all_to_all(copies, "dp", 0, 0, tiled=True).reshape(-1, BLOCK, BLOCK)
    out, at = [], 0
    for shape in shapes:
        out.append(whole[at:at + shape[0]].astype(jnp.float32))
        at += shape[0]
    return tuple(out)


def mp_sum(v):
    n = lax.axis_size("mp")
    v = v + lax.ppermute(v, "mp", [(i, i ^ 1) for i in range(n)])
    return v + lax.ppermute(v, "mp", [(i, i ^ 2) for i in range(n)])


def pair_major(blocks):
    n, c, _ = blocks.shape
    return blocks.reshape(n, c, NBLK, 2).transpose(0, 1, 3, 2).reshape(n, c, 2 * NBLK)


def pair_minor(blocks):
    n, c, _ = blocks.shape
    return blocks.reshape(n, c, 2, NBLK).transpose(0, 1, 3, 2).reshape(n, c, 2 * NBLK)


def body(samples, gain, left_blocks, gate_blocks, right_blocks, cotangent):
    rows, width_local = samples.shape
    nlocal = left_blocks.shape[0]
    xf = samples.astype(jnp.float32)
    cot_blocks = cotangent.reshape(rows, nlocal, BLOCK)
    grad_perm = jnp.einsum(
        "tkm,kcm->tkc", cot_blocks, right_blocks, preferred_element_type=jnp.float32
    ).astype(jnp.bfloat16)
    squares = mp_sum(jnp.sum(xf * xf, axis=1))
    grad_perm, squares = lax.optimization_barrier((grad_perm, squares))
    rstd = lax.rsqrt(squares / W + 1e-05)[:, None]
    xn = (xf * rstd * gain).astype(jnp.bfloat16).reshape(rows, nlocal, BLOCK)
    left_p = pair_major(left_blocks)
    gate_p = pair_major(gate_blocks)
    act_a = jnp.einsum("tic,icj->tij", xn, left_p, preferred_element_type=jnp.float32)
    act_g = jnp.einsum("tic,icj->tij", xn, gate_p, preferred_element_type=jnp.float32)
    gated = (act_a * jax.nn.silu(act_g)).astype(jnp.bfloat16)
    outgoing = (
        gated.reshape(rows, nlocal, 2, NBLK).transpose(0, 3, 1, 2).reshape(rows, NBLK, 2 * nlocal)
    )
    returned = lax.all_to_all(grad_perm, "mp", split_axis=2, concat_axis=1, tiled=True)
    outgoing, xn_b = lax.optimization_barrier((outgoing, xn))
    permuted = lax.all_to_all(outgoing, "mp", split_axis=1, concat_axis=2, tiled=True)
    act_a = jnp.einsum("tic,icj->tij", xn_b, left_p, preferred_element_type=jnp.float32)
    act_g = jnp.einsum("tic,icj->tij", xn_b, gate_p, preferred_element_type=jnp.float32)
    silu_g = jax.nn.silu(act_g)
    grad_gated = (
        returned.reshape(rows, NBLK, nlocal, 2)
        .transpose(0, 2, 3, 1)
        .reshape(rows, nlocal, BLOCK)
        .astype(jnp.float32)
    )
    sigma = jax.nn.sigmoid(act_g)
    grad_a = (grad_gated * silu_g).astype(jnp.bfloat16)
    grad_g = (grad_gated * act_a * sigma * (1.0 + act_g * (1.0 - sigma))).astype(jnp.bfloat16)
    left_local = pair_minor(jnp.einsum("tic,tij->icj", xn_b, grad_a, preferred_element_type=jnp.float32))
    gate_local = pair_minor(jnp.einsum("tic,tij->icj", xn_b, grad_g, preferred_element_type=jnp.float32))
    grad_norm = jnp.einsum("tij,icj->tic", grad_a, left_p, preferred_element_type=jnp.float32)
    grad_norm = grad_norm + jnp.einsum(
        "tij,icj->tic", grad_g, gate_p, preferred_element_type=jnp.float32
    )
    permuted, left_local, gate_local, grad_norm = lax.optimization_barrier(
        (permuted, left_local, gate_local, grad_norm)
    )
    right_local = jnp.einsum(
        "tkc,tkm->kcm", permuted, cot_blocks, preferred_element_type=jnp.float32
    )
    partials = (left_local, gate_local, right_local)
    mine = dp_reduce_scatter(partials)
    scaled = grad_norm.reshape(rows, width_local) * gain
    inner = mp_sum(jnp.sum(scaled * xf, axis=1))
    mine, inner = lax.optimization_barrier((mine, inner))
    mean_inner = (inner / W)[:, None]
    grad_input = (
        cotangent.astype(jnp.float32) + rstd * (scaled - xf * rstd * rstd * mean_inner)
    ).astype(jnp.bfloat16)
    left_total, gate_total, right_total = dp_all_gather(mine, [p.shape for p in partials])
    return (grad_input, left_total, gate_total, right_total)


def solution(mesh):
    placed = (
        P("dp", "mp"),
        P("mp"),
        P("mp", None, None),
        P("mp", None, None),
        P("mp", None, None),
        P("dp", "mp"),
    )
    return jax.shard_map(
        body,
        mesh=mesh,
        in_specs=placed,
        out_specs=(P("dp", "mp"), P("mp", None, None), P("mp", None, None), P("mp", None, None)),
        check_vma=False,
    )
```

```python
import jax
import jax.numpy as jnp
from jax import lax
from jax.sharding import PartitionSpec as P

W = 8192
BLOCK = 128
NBLK = 64


HALVING_BITS = (0, 2, 1, 3, 4)


def dp_halving_sum(flat):
    me = lax.axis_index("dp")
    ndp = lax.axis_size("dp")
    for b in HALVING_BITS:
        bit = (me >> b) & 1
        lo, hi = jnp.split(flat, 2)
        keep = jnp.where(bit == 0, lo, hi)
        send = jnp.where(bit == 0, hi, lo)
        flat = keep + lax.ppermute(send, "dp", [(i, i ^ (1 << b)) for i in range(ndp)])
    return flat


def halving_order(gathered):
    nb = len(HALVING_BITS)
    view = gathered.reshape((2,) * nb + gathered.shape[1:])
    axes = [nb - 1 - b for b in HALVING_BITS]
    return view.transpose(axes + list(range(nb, view.ndim))).reshape(gathered.shape)


def dp_reduce_scatter(parts):
    ndp = lax.axis_size("dp")
    flat = jnp.concatenate([p.reshape(-1, BLOCK) for p in parts]).reshape(ndp, -1, BLOCK)
    got = lax.all_to_all(flat, "dp", 0, 0, tiled=True)
    return jnp.sum(got, axis=0)


def dp_all_gather(mine):
    ndp = lax.axis_size("dp")
    copies = jnp.broadcast_to(mine.astype(jnp.bfloat16)[None], (ndp,) + mine.shape)
    return lax.all_to_all(copies, "dp", 0, 0, tiled=True)


def pair_major(blocks):
    n, c, _ = blocks.shape
    return blocks.reshape(n, c, NBLK, 2).transpose(0, 1, 3, 2).reshape(n, c, 2 * NBLK)


def pair_minor(blocks):
    n, c, _ = blocks.shape
    return blocks.reshape(n, c, 2, NBLK).transpose(0, 1, 3, 2).reshape(n, c, 2 * NBLK)


def body(samples, gain, left_blocks, gate_blocks, right_blocks, cotangent):
    rows, width_local = samples.shape
    nlocal = left_blocks.shape[0]
    xf = samples.astype(jnp.float32)
    cot_blocks = cotangent.reshape(rows, nlocal, BLOCK)
    grad_perm = jnp.einsum(
        "tkm,kcm->tkc", cot_blocks, right_blocks, preferred_element_type=jnp.float32
    ).astype(jnp.bfloat16)
    squares = lax.psum(jnp.sum(xf * xf, axis=1), "mp")
    grad_perm, squares = lax.optimization_barrier((grad_perm, squares))
    rstd = lax.rsqrt(squares / W + 1e-05)[:, None]
    xn = (xf * rstd * gain).astype(jnp.bfloat16).reshape(rows, nlocal, BLOCK)
    left_p = pair_major(left_blocks)
    gate_p = pair_major(gate_blocks)
    act_a = jnp.einsum("tic,icj->tij", xn, left_p, preferred_element_type=jnp.float32)
    act_g = jnp.einsum("tic,icj->tij", xn, gate_p, preferred_element_type=jnp.float32)
    gated = (act_a * jax.nn.silu(act_g)).astype(jnp.bfloat16)
    outgoing = (
        gated.reshape(rows, nlocal, 2, NBLK).transpose(0, 3, 1, 2).reshape(rows, NBLK, 2 * nlocal)
    )
    returned = lax.all_to_all(grad_perm, "mp", split_axis=2, concat_axis=1, tiled=True)
    outgoing, xn_b = lax.optimization_barrier((outgoing, xn))
    permuted = lax.all_to_all(outgoing, "mp", split_axis=1, concat_axis=2, tiled=True)
    act_a = jnp.einsum("tic,icj->tij", xn_b, left_p, preferred_element_type=jnp.float32)
    act_g = jnp.einsum("tic,icj->tij", xn_b, gate_p, preferred_element_type=jnp.float32)
    silu_g = jax.nn.silu(act_g)
    grad_gated = (
        returned.reshape(rows, NBLK, nlocal, 2)
        .transpose(0, 2, 3, 1)
        .reshape(rows, nlocal, BLOCK)
        .astype(jnp.float32)
    )
    sigma = jax.nn.sigmoid(act_g)
    grad_a = (grad_gated * silu_g).astype(jnp.bfloat16)
    grad_g = (grad_gated * act_a * sigma * (1.0 + act_g * (1.0 - sigma))).astype(jnp.bfloat16)
    left_local = pair_minor(jnp.einsum("tic,tij->icj", xn_b, grad_a, preferred_element_type=jnp.float32))
    gate_local = pair_minor(jnp.einsum("tic,tij->icj", xn_b, grad_g, preferred_element_type=jnp.float32))
    grad_norm = jnp.einsum("tij,icj->tic", grad_a, left_p, preferred_element_type=jnp.float32)
    grad_norm = grad_norm + jnp.einsum(
        "tij,icj->tic", grad_g, gate_p, preferred_element_type=jnp.float32
    )
    lg_mine = dp_halving_sum(jnp.concatenate([left_local.reshape(-1, BLOCK), gate_local.reshape(-1, BLOCK)]))
    permuted, grad_norm = lax.optimization_barrier((permuted, grad_norm))
    right_local = jnp.einsum(
        "tkc,tkm->kcm", permuted, cot_blocks, preferred_element_type=jnp.float32
    )
    right_mine = dp_reduce_scatter((right_local,))
    mine = jnp.concatenate([lg_mine, right_mine])
    scaled = grad_norm.reshape(rows, width_local) * gain
    inner = lax.psum(jnp.sum(scaled * xf, axis=1), "mp")
    mean_inner = (inner / W)[:, None]
    grad_input = (
        cotangent.astype(jnp.float32) + rstd * (scaled - xf * rstd * rstd * mean_inner)
    ).astype(jnp.bfloat16)
    mine, grad_input = lax.optimization_barrier((mine, grad_input))
    whole = dp_all_gather(mine)
    nlg = lg_mine.shape[0]
    lg = halving_order(whole[:, :nlg]).reshape(2, nlocal, BLOCK, BLOCK).astype(jnp.float32)
    left_total, gate_total = lg[0], lg[1]
    right_total = whole[:, nlg:].reshape(nlocal, BLOCK, BLOCK).astype(jnp.float32)
    return (grad_input, left_total, gate_total, right_total)


def solution(mesh):
    placed = (
        P("dp", "mp"),
        P("mp"),
        P("mp", None, None),
        P("mp", None, None),
        P("mp", None, None),
        P("dp", "mp"),
    )
    return jax.shard_map(
        body,
        mesh=mesh,
        in_specs=placed,
        out_specs=(P("dp", "mp"), P("mp", None, None), P("mp", None, None), P("mp", None, None)),
        check_vma=False,
    )
```

```python
import jax
import jax.numpy as jnp
from jax import lax
from jax.sharding import PartitionSpec as P

W = 8192
BLOCK = 128
NBLK = 64


HALVING_BITS = (0, 2, 1, 3, 4)


def dp_halving_sum(flat):
    me = lax.axis_index("dp")
    ndp = lax.axis_size("dp")
    for b in HALVING_BITS:
        bit = (me >> b) & 1
        lo, hi = jnp.split(flat, 2)
        keep = jnp.where(bit == 0, lo, hi)
        send = jnp.where(bit == 0, hi, lo)
        flat = keep + lax.ppermute(send, "dp", [(i, i ^ (1 << b)) for i in range(ndp)])
    return flat


def halving_order(gathered):
    nb = len(HALVING_BITS)
    view = gathered.reshape((2,) * nb + gathered.shape[1:])
    axes = [nb - 1 - b for b in HALVING_BITS]
    return view.transpose(axes + list(range(nb, view.ndim))).reshape(gathered.shape)


def dp_reduce_scatter(parts):
    ndp = lax.axis_size("dp")
    flat = jnp.concatenate([p.reshape(-1, BLOCK) for p in parts]).reshape(ndp, -1, BLOCK)
    got = lax.all_to_all(flat, "dp", 0, 0, tiled=True)
    return jnp.sum(got, axis=0)


def dp_all_gather(mine):
    ndp = lax.axis_size("dp")
    copies = jnp.broadcast_to(mine.astype(jnp.bfloat16)[None], (ndp,) + mine.shape)
    return lax.all_to_all(copies, "dp", 0, 0, tiled=True)


def pair_major(blocks):
    n, c, _ = blocks.shape
    return blocks.reshape(n, c, NBLK, 2).transpose(0, 1, 3, 2).reshape(n, c, 2 * NBLK)


def pair_minor(blocks):
    n, c, _ = blocks.shape
    return blocks.reshape(n, c, 2, NBLK).transpose(0, 1, 3, 2).reshape(n, c, 2 * NBLK)


def body(samples, gain, left_blocks, gate_blocks, right_blocks, cotangent):
    rows, width_local = samples.shape
    nlocal = left_blocks.shape[0]
    xf = samples.astype(jnp.float32)
    cot_blocks = cotangent.reshape(rows, nlocal, BLOCK)
    grad_perm = jnp.einsum(
        "tkm,kcm->tkc", cot_blocks, right_blocks, preferred_element_type=jnp.float32
    ).astype(jnp.bfloat16)
    squares = lax.psum(jnp.sum(xf * xf, axis=1), "mp")
    grad_perm, squares = lax.optimization_barrier((grad_perm, squares))
    rstd = lax.rsqrt(squares / W + 1e-05)[:, None]
    xn = (xf * rstd * gain).astype(jnp.bfloat16).reshape(rows, nlocal, BLOCK)
    left_p = pair_major(left_blocks)
    gate_p = pair_major(gate_blocks)
    act_a = jnp.einsum("tic,icj->tij", xn, left_p, preferred_element_type=jnp.float32)
    act_g = jnp.einsum("tic,icj->tij", xn, gate_p, preferred_element_type=jnp.float32)
    gated = (act_a * jax.nn.silu(act_g)).astype(jnp.bfloat16)
    outgoing = (
        gated.reshape(rows, nlocal, 2, NBLK).transpose(0, 3, 1, 2).reshape(rows, NBLK, 2 * nlocal)
    )
    returned = lax.all_to_all(grad_perm, "mp", split_axis=2, concat_axis=1, tiled=True)
    outgoing, xn_b = lax.optimization_barrier((outgoing, xn))
    permuted = lax.all_to_all(outgoing, "mp", split_axis=1, concat_axis=2, tiled=True)
    act_a = jnp.einsum("tic,icj->tij", xn_b, left_p, preferred_element_type=jnp.float32)
    act_g = jnp.einsum("tic,icj->tij", xn_b, gate_p, preferred_element_type=jnp.float32)
    silu_g = jax.nn.silu(act_g)
    grad_gated = (
        returned.reshape(rows, NBLK, nlocal, 2)
        .transpose(0, 2, 3, 1)
        .reshape(rows, nlocal, BLOCK)
        .astype(jnp.float32)
    )
    sigma = jax.nn.sigmoid(act_g)
    grad_a = (grad_gated * silu_g).astype(jnp.bfloat16)
    grad_g = (grad_gated * act_a * sigma * (1.0 + act_g * (1.0 - sigma))).astype(jnp.bfloat16)
    left_local = pair_minor(jnp.einsum("tic,tij->icj", xn_b, grad_a, preferred_element_type=jnp.float32))
    gate_local = pair_minor(jnp.einsum("tic,tij->icj", xn_b, grad_g, preferred_element_type=jnp.float32))
    grad_norm = jnp.einsum("tij,icj->tic", grad_a, left_p, preferred_element_type=jnp.float32)
    grad_norm = grad_norm + jnp.einsum(
        "tij,icj->tic", grad_g, gate_p, preferred_element_type=jnp.float32
    )
    permuted, left_local, gate_local, grad_norm = lax.optimization_barrier(
        (permuted, left_local, gate_local, grad_norm)
    )
    lg_mine = dp_halving_sum(jnp.concatenate([left_local.reshape(-1, BLOCK), gate_local.reshape(-1, BLOCK)]))
    right_local = jnp.einsum(
        "tkc,tkm->kcm", permuted, cot_blocks, preferred_element_type=jnp.float32
    )
    right_mine = dp_reduce_scatter((right_local,))
    mine = jnp.concatenate([lg_mine, right_mine])
    scaled = grad_norm.reshape(rows, width_local) * gain
    inner = lax.psum(jnp.sum(scaled * xf, axis=1), "mp")
    mean_inner = (inner / W)[:, None]
    grad_input = (
        cotangent.astype(jnp.float32) + rstd * (scaled - xf * rstd * rstd * mean_inner)
    ).astype(jnp.bfloat16)
    mine, grad_input = lax.optimization_barrier((mine, grad_input))
    whole = dp_all_gather(mine)
    nlg = lg_mine.shape[0]
    lg = halving_order(whole[:, :nlg]).reshape(2, nlocal, BLOCK, BLOCK).astype(jnp.float32)
    left_total, gate_total = lg[0], lg[1]
    right_total = whole[:, nlg:].reshape(nlocal, BLOCK, BLOCK).astype(jnp.float32)
    return (grad_input, left_total, gate_total, right_total)


def solution(mesh):
    placed = (
        P("dp", "mp"),
        P("mp"),
        P("mp", None, None),
        P("mp", None, None),
        P("mp", None, None),
        P("dp", "mp"),
    )
    return jax.shard_map(
        body,
        mesh=mesh,
        in_specs=placed,
        out_specs=(P("dp", "mp"), P("mp", None, None), P("mp", None, None), P("mp", None, None)),
        check_vma=False,
    )
```

```python
import jax
import jax.numpy as jnp
from jax import lax
from jax.sharding import PartitionSpec as P

W = 8192
BLOCK = 128
NBLK = 64


def dp_reduce_scatter(parts):
    ndp = lax.axis_size("dp")
    flat = jnp.concatenate([p.reshape(-1, BLOCK) for p in parts]).reshape(ndp, -1, BLOCK)
    got = lax.all_to_all(flat, "dp", 0, 0, tiled=True)
    return jnp.sum(got, axis=0)


def dp_all_gather(mine, shapes):
    ndp = lax.axis_size("dp")
    copies = jnp.broadcast_to(mine.astype(jnp.bfloat16)[None], (ndp,) + mine.shape)
    whole = lax.all_to_all(copies, "dp", 0, 0, tiled=True).reshape(-1, BLOCK, BLOCK)
    out, at = [], 0
    for shape in shapes:
        out.append(whole[at:at + shape[0]].astype(jnp.float32))
        at += shape[0]
    return tuple(out)


def pair_major(blocks):
    n, c, _ = blocks.shape
    return blocks.reshape(n, c, NBLK, 2).transpose(0, 1, 3, 2).reshape(n, c, 2 * NBLK)


def pair_minor(blocks):
    n, c, _ = blocks.shape
    return blocks.reshape(n, c, 2, NBLK).transpose(0, 1, 3, 2).reshape(n, c, 2 * NBLK)


def body(samples, gain, left_blocks, gate_blocks, right_blocks, cotangent):
    rows, width_local = samples.shape
    nlocal = left_blocks.shape[0]
    xf = samples.astype(jnp.float32)
    cot_blocks = cotangent.reshape(rows, nlocal, BLOCK)
    grad_perm = jnp.einsum(
        "tkm,kcm->tkc", cot_blocks, right_blocks, preferred_element_type=jnp.float32
    ).astype(jnp.bfloat16)
    squares = lax.psum(jnp.sum(xf * xf, axis=1), "mp")
    rstd = lax.rsqrt(squares / W + 1e-05)[:, None]
    xn = (xf * rstd * gain).astype(jnp.bfloat16).reshape(rows, nlocal, BLOCK)
    left_p = pair_major(left_blocks)
    gate_p = pair_major(gate_blocks)
    act_a = jnp.einsum("tic,icj->tij", xn, left_p, preferred_element_type=jnp.float32)
    act_g = jnp.einsum("tic,icj->tij", xn, gate_p, preferred_element_type=jnp.float32)
    gated = (act_a * jax.nn.silu(act_g)).astype(jnp.bfloat16)
    outgoing = (
        gated.reshape(rows, nlocal, 2, NBLK).transpose(0, 3, 1, 2).reshape(rows, NBLK, 2 * nlocal)
    )
    returned = lax.all_to_all(grad_perm, "mp", split_axis=2, concat_axis=1, tiled=True)
    outgoing, xn_b = lax.optimization_barrier((outgoing, xn))
    permuted = lax.all_to_all(outgoing, "mp", split_axis=1, concat_axis=2, tiled=True)
    act_a = jnp.einsum("tic,icj->tij", xn_b, left_p, preferred_element_type=jnp.float32)
    act_g = jnp.einsum("tic,icj->tij", xn_b, gate_p, preferred_element_type=jnp.float32)
    silu_g = jax.nn.silu(act_g)
    grad_gated = (
        returned.reshape(rows, NBLK, nlocal, 2)
        .transpose(0, 2, 3, 1)
        .reshape(rows, nlocal, BLOCK)
        .astype(jnp.float32)
    )
    sigma = jax.nn.sigmoid(act_g)
    grad_a = (grad_gated * silu_g).astype(jnp.bfloat16)
    grad_g = (grad_gated * act_a * sigma * (1.0 + act_g * (1.0 - sigma))).astype(jnp.bfloat16)
    left_local = pair_minor(jnp.einsum("tic,tij->icj", xn_b, grad_a, preferred_element_type=jnp.float32))
    gate_local = pair_minor(jnp.einsum("tic,tij->icj", xn_b, grad_g, preferred_element_type=jnp.float32))
    grad_norm = jnp.einsum("tij,icj->tic", grad_a, left_p, preferred_element_type=jnp.float32)
    grad_norm = grad_norm + jnp.einsum(
        "tij,icj->tic", grad_g, gate_p, preferred_element_type=jnp.float32
    )
    permuted, left_local, gate_local, grad_norm = lax.optimization_barrier(
        (permuted, left_local, gate_local, grad_norm)
    )
    right_local = jnp.einsum(
        "tkc,tkm->kcm", permuted, cot_blocks, preferred_element_type=jnp.float32
    )
    partials = (left_local, gate_local, right_local)
    mine = dp_reduce_scatter(partials)
    scaled = grad_norm.reshape(rows, width_local) * gain
    inner = lax.psum(jnp.sum(scaled * xf, axis=1), "mp")
    mean_inner = (inner / W)[:, None]
    grad_input = (
        cotangent.astype(jnp.float32) + rstd * (scaled - xf * rstd * rstd * mean_inner)
    ).astype(jnp.bfloat16)
    mine, grad_input = lax.optimization_barrier((mine, grad_input))
    left_total, gate_total, right_total = dp_all_gather(mine, [p.shape for p in partials])
    return (grad_input, left_total, gate_total, right_total)


def solution(mesh):
    placed = (
        P("dp", "mp"),
        P("mp"),
        P("mp", None, None),
        P("mp", None, None),
        P("mp", None, None),
        P("dp", "mp"),
    )
    return jax.shard_map(
        body,
        mesh=mesh,
        in_specs=placed,
        out_specs=(P("dp", "mp"), P("mp", None, None), P("mp", None, None), P("mp", None, None)),
        check_vma=False,
    )
```

```python
import jax
import jax.numpy as jnp
from jax import lax
from jax.sharding import PartitionSpec as P

W = 8192
BLOCK = 128
NBLK = 64


def dp_reduce_scatter(parts):
    ndp = lax.axis_size("dp")
    flat = jnp.concatenate([p.reshape(-1, BLOCK) for p in parts]).reshape(ndp, -1, BLOCK)
    got = lax.all_to_all(flat, "dp", 0, 0, tiled=True)
    return jnp.sum(got, axis=0)


def dp_all_gather(mine, shapes):
    ndp = lax.axis_size("dp")
    copies = jnp.broadcast_to(mine.astype(jnp.bfloat16)[None], (ndp,) + mine.shape)
    whole = lax.all_to_all(copies, "dp", 0, 0, tiled=True).reshape(-1, BLOCK, BLOCK)
    out, at = [], 0
    for shape in shapes:
        out.append(whole[at:at + shape[0]].astype(jnp.float32))
        at += shape[0]
    return tuple(out)


def pair_major(blocks):
    n, c, _ = blocks.shape
    return blocks.reshape(n, c, NBLK, 2).transpose(0, 1, 3, 2).reshape(n, c, 2 * NBLK)


def pair_minor(blocks):
    n, c, _ = blocks.shape
    return blocks.reshape(n, c, 2, NBLK).transpose(0, 1, 3, 2).reshape(n, c, 2 * NBLK)


def body(samples, gain, left_blocks, gate_blocks, right_blocks, cotangent):
    rows, width_local = samples.shape
    nlocal = left_blocks.shape[0]
    xf = samples.astype(jnp.float32)
    cot_blocks = cotangent.reshape(rows, nlocal, BLOCK)
    grad_perm = jnp.einsum(
        "tkm,kcm->tkc", cot_blocks, right_blocks, preferred_element_type=jnp.float32
    ).astype(jnp.bfloat16)
    squares = lax.psum(jnp.sum(xf * xf, axis=1), "mp")
    grad_perm, squares = lax.optimization_barrier((grad_perm, squares))
    rstd = lax.rsqrt(squares / W + 1e-05)[:, None]
    xn = (xf * rstd * gain).astype(jnp.bfloat16).reshape(rows, nlocal, BLOCK)
    left_p = pair_major(left_blocks)
    gate_p = pair_major(gate_blocks)
    act_a = jnp.einsum("tic,icj->tij", xn, left_p, preferred_element_type=jnp.float32)
    act_g = jnp.einsum("tic,icj->tij", xn, gate_p, preferred_element_type=jnp.float32)
    gated = (act_a * jax.nn.silu(act_g)).astype(jnp.bfloat16)
    outgoing = (
        gated.reshape(rows, nlocal, 2, NBLK).transpose(0, 3, 1, 2).reshape(rows, NBLK, 2 * nlocal)
    )
    returned = lax.all_to_all(grad_perm, "mp", split_axis=2, concat_axis=1, tiled=True)
    outgoing, xn_b = lax.optimization_barrier((outgoing, xn))
    me = lax.axis_index("mp")
    nmp = lax.axis_size("mp")
    width = outgoing.shape[1] // nmp
    arrived = [lax.dynamic_slice_in_dim(outgoing, me * width, width, axis=1)]
    for d in range(1, nmp):
        chunk = lax.dynamic_slice_in_dim(outgoing, (me ^ d) * width, width, axis=1)
        arrived.append(lax.ppermute(chunk, "mp", [(i, i ^ d) for i in range(nmp)]))
    act_a = jnp.einsum("tic,icj->tij", xn_b, left_p, preferred_element_type=jnp.float32)
    act_g = jnp.einsum("tic,icj->tij", xn_b, gate_p, preferred_element_type=jnp.float32)
    silu_g = jax.nn.silu(act_g)
    grad_gated = (
        returned.reshape(rows, NBLK, nlocal, 2)
        .transpose(0, 2, 3, 1)
        .reshape(rows, nlocal, BLOCK)
        .astype(jnp.float32)
    )
    sigma = jax.nn.sigmoid(act_g)
    grad_a = (grad_gated * silu_g).astype(jnp.bfloat16)
    grad_g = (grad_gated * act_a * sigma * (1.0 + act_g * (1.0 - sigma))).astype(jnp.bfloat16)
    left_local = pair_minor(jnp.einsum("tic,tij->icj", xn_b, grad_a, preferred_element_type=jnp.float32))
    gate_local = pair_minor(jnp.einsum("tic,tij->icj", xn_b, grad_g, preferred_element_type=jnp.float32))
    grad_norm = jnp.einsum("tij,icj->tic", grad_a, left_p, preferred_element_type=jnp.float32)
    grad_norm = grad_norm + jnp.einsum(
        "tij,icj->tic", grad_g, gate_p, preferred_element_type=jnp.float32
    )
    lg_mine = dp_reduce_scatter((left_local, gate_local))
    arrived, grad_norm = lax.optimization_barrier((arrived, grad_norm))
    permuted = jnp.stack(arrived, axis=2).reshape(rows, nlocal, BLOCK)
    by_partner = jnp.einsum(
        "tkc,tkm->kcm", permuted, cot_blocks, preferred_element_type=jnp.float32
    ).reshape(nlocal, nmp, BLOCK // nmp, BLOCK)
    right_local = jnp.concatenate(
        [lax.dynamic_index_in_dim(by_partner, me ^ b, axis=1, keepdims=False) for b in range(nmp)], axis=1
    )
    right_mine = dp_reduce_scatter((right_local,))
    mine = jnp.concatenate([lg_mine, right_mine])
    scaled = grad_norm.reshape(rows, width_local) * gain
    inner = lax.psum(jnp.sum(scaled * xf, axis=1), "mp")
    mean_inner = (inner / W)[:, None]
    grad_input = (
        cotangent.astype(jnp.float32) + rstd * (scaled - xf * rstd * rstd * mean_inner)
    ).astype(jnp.bfloat16)
    mine, grad_input = lax.optimization_barrier((mine, grad_input))
    ndp = lax.axis_size("dp")
    whole = lax.all_to_all(
        jnp.broadcast_to(mine.astype(jnp.bfloat16)[None], (ndp,) + mine.shape), "dp", 0, 0, tiled=True
    )
    nlg = lg_mine.shape[0]
    lg = whole[:, :nlg].reshape(2, nlocal, BLOCK, BLOCK).astype(jnp.float32)
    left_total, gate_total = lg[0], lg[1]
    right_total = whole[:, nlg:].reshape(nlocal, BLOCK, BLOCK).astype(jnp.float32)
    return (grad_input, left_total, gate_total, right_total)


def solution(mesh):
    placed = (
        P("dp", "mp"),
        P("mp"),
        P("mp", None, None),
        P("mp", None, None),
        P("mp", None, None),
        P("dp", "mp"),
    )
    return jax.shard_map(
        body,
        mesh=mesh,
        in_specs=placed,
        out_specs=(P("dp", "mp"), P("mp", None, None), P("mp", None, None), P("mp", None, None)),
        check_vma=False,
    )
```

```python
import jax
import jax.numpy as jnp
from jax import lax
from jax.sharding import PartitionSpec as P

W = 8192
BLOCK = 128
NBLK = 64


def dp_reduce_scatter(parts):
    ndp = lax.axis_size("dp")
    flat = jnp.concatenate([p.reshape(-1, BLOCK) for p in parts]).reshape(ndp, -1, BLOCK)
    got = lax.all_to_all(flat, "dp", 0, 0, tiled=True)
    return jnp.sum(got, axis=0)


def dp_all_gather(mine, shapes):
    ndp = lax.axis_size("dp")
    copies = jnp.broadcast_to(mine.astype(jnp.bfloat16)[None], (ndp,) + mine.shape)
    whole = lax.all_to_all(copies, "dp", 0, 0, tiled=True).reshape(-1, BLOCK, BLOCK)
    out, at = [], 0
    for shape in shapes:
        out.append(whole[at:at + shape[0]].astype(jnp.float32))
        at += shape[0]
    return tuple(out)


def pair_major(blocks):
    n, c, _ = blocks.shape
    return blocks.reshape(n, c, NBLK, 2).transpose(0, 1, 3, 2).reshape(n, c, 2 * NBLK)


def pair_minor(blocks):
    n, c, _ = blocks.shape
    return blocks.reshape(n, c, 2, NBLK).transpose(0, 1, 3, 2).reshape(n, c, 2 * NBLK)


def body(samples, gain, left_blocks, gate_blocks, right_blocks, cotangent):
    rows, width_local = samples.shape
    nlocal = left_blocks.shape[0]
    xf = samples.astype(jnp.float32)
    cot_blocks = cotangent.reshape(rows, nlocal, BLOCK)
    grad_perm = jnp.einsum(
        "tkm,kcm->tkc", cot_blocks, right_blocks, preferred_element_type=jnp.float32
    ).astype(jnp.bfloat16)
    squares = lax.psum(jnp.sum(xf * xf, axis=1), "mp")
    grad_perm, squares = lax.optimization_barrier((grad_perm, squares))
    rstd = lax.rsqrt(squares / W + 1e-05)[:, None]
    xn = (xf * rstd * gain).astype(jnp.bfloat16).reshape(rows, nlocal, BLOCK)
    left_p = pair_major(left_blocks)
    gate_p = pair_major(gate_blocks)
    act_a = jnp.einsum("tic,icj->tij", xn, left_p, preferred_element_type=jnp.float32)
    act_g = jnp.einsum("tic,icj->tij", xn, gate_p, preferred_element_type=jnp.float32)
    gated = (act_a * jax.nn.silu(act_g)).astype(jnp.bfloat16)
    outgoing = (
        gated.reshape(rows, nlocal, 2, NBLK).transpose(0, 3, 1, 2).reshape(rows, NBLK, 2 * nlocal)
    )
    returned = lax.all_to_all(grad_perm, "mp", split_axis=2, concat_axis=1, tiled=True)
    outgoing, xn_b = lax.optimization_barrier((outgoing, xn))
    me = lax.axis_index("mp")
    nmp = lax.axis_size("mp")
    width = outgoing.shape[1] // nmp
    arrived = [lax.dynamic_slice_in_dim(outgoing, me * width, width, axis=1)]
    for d in range(1, nmp):
        chunk = lax.dynamic_slice_in_dim(outgoing, (me ^ d) * width, width, axis=1)
        arrived.append(lax.ppermute(chunk, "mp", [(i, i ^ d) for i in range(nmp)]))
    act_a = jnp.einsum("tic,icj->tij", xn_b, left_p, preferred_element_type=jnp.float32)
    act_g = jnp.einsum("tic,icj->tij", xn_b, gate_p, preferred_element_type=jnp.float32)
    silu_g = jax.nn.silu(act_g)
    grad_gated = (
        returned.reshape(rows, NBLK, nlocal, 2)
        .transpose(0, 2, 3, 1)
        .reshape(rows, nlocal, BLOCK)
        .astype(jnp.float32)
    )
    sigma = jax.nn.sigmoid(act_g)
    grad_a = (grad_gated * silu_g).astype(jnp.bfloat16)
    grad_g = (grad_gated * act_a * sigma * (1.0 + act_g * (1.0 - sigma))).astype(jnp.bfloat16)
    left_local = pair_minor(jnp.einsum("tic,tij->icj", xn_b, grad_a, preferred_element_type=jnp.float32))
    gate_local = pair_minor(jnp.einsum("tic,tij->icj", xn_b, grad_g, preferred_element_type=jnp.float32))
    grad_norm = jnp.einsum("tij,icj->tic", grad_a, left_p, preferred_element_type=jnp.float32)
    grad_norm = grad_norm + jnp.einsum(
        "tij,icj->tic", grad_g, gate_p, preferred_element_type=jnp.float32
    )
    arrived, left_local, gate_local, grad_norm = lax.optimization_barrier(
        (arrived, left_local, gate_local, grad_norm)
    )
    permuted = jnp.stack(arrived, axis=2).reshape(rows, nlocal, BLOCK)
    by_partner = jnp.einsum(
        "tkc,tkm->kcm", permuted, cot_blocks, preferred_element_type=jnp.float32
    ).reshape(nlocal, nmp, BLOCK // nmp, BLOCK)
    right_local = jnp.concatenate(
        [lax.dynamic_index_in_dim(by_partner, me ^ b, axis=1, keepdims=False) for b in range(nmp)], axis=1
    )
    partials = (left_local, gate_local, right_local)
    mine = dp_reduce_scatter(partials)
    scaled = grad_norm.reshape(rows, width_local) * gain
    inner = lax.psum(jnp.sum(scaled * xf, axis=1), "mp")
    mean_inner = (inner / W)[:, None]
    grad_input = (
        cotangent.astype(jnp.float32) + rstd * (scaled - xf * rstd * rstd * mean_inner)
    ).astype(jnp.bfloat16)
    mine, grad_input = lax.optimization_barrier((mine, grad_input))
    left_total, gate_total, right_total = dp_all_gather(mine, [p.shape for p in partials])
    return (grad_input, left_total, gate_total, right_total)


def solution(mesh):
    placed = (
        P("dp", "mp"),
        P("mp"),
        P("mp", None, None),
        P("mp", None, None),
        P("mp", None, None),
        P("dp", "mp"),
    )
    return jax.shard_map(
        body,
        mesh=mesh,
        in_specs=placed,
        out_specs=(P("dp", "mp"), P("mp", None, None), P("mp", None, None), P("mp", None, None)),
        check_vma=False,
    )
```

```python
import jax
import jax.numpy as jnp
from jax import lax
from jax.sharding import PartitionSpec as P

W = 8192
BLOCK = 128
NBLK = 64


def dp_reduce_scatter(parts):
    ndp = lax.axis_size("dp")
    flat = jnp.concatenate([p.reshape(-1, BLOCK) for p in parts]).reshape(ndp, -1, BLOCK)
    got = lax.all_to_all(flat, "dp", 0, 0, tiled=True)
    return jnp.sum(got, axis=0)


def dp_all_gather(mine, shapes):
    ndp = lax.axis_size("dp")
    copies = jnp.broadcast_to(mine.astype(jnp.bfloat16)[None], (ndp,) + mine.shape)
    whole = lax.all_to_all(copies, "dp", 0, 0, tiled=True).reshape(-1, BLOCK, BLOCK)
    out, at = [], 0
    for shape in shapes:
        out.append(whole[at:at + shape[0]].astype(jnp.float32))
        at += shape[0]
    return tuple(out)


def pair_major(blocks):
    n, c, _ = blocks.shape
    return blocks.reshape(n, c, NBLK, 2).transpose(0, 1, 3, 2).reshape(n, c, 2 * NBLK)


def pair_minor(blocks):
    n, c, _ = blocks.shape
    return blocks.reshape(n, c, 2, NBLK).transpose(0, 1, 3, 2).reshape(n, c, 2 * NBLK)


def body(samples, gain, left_blocks, gate_blocks, right_blocks, cotangent):
    rows, width_local = samples.shape
    nlocal = left_blocks.shape[0]
    xf = samples.astype(jnp.float32)
    cot_blocks = cotangent.reshape(rows, nlocal, BLOCK)
    grad_perm = jnp.einsum(
        "tkm,kcm->tkc", cot_blocks, right_blocks, preferred_element_type=jnp.float32
    ).astype(jnp.bfloat16)
    squares = lax.psum(jnp.sum(xf * xf, axis=1), "mp")
    grad_perm, squares = lax.optimization_barrier((grad_perm, squares))
    rstd = lax.rsqrt(squares / W + 1e-05)[:, None]
    xn = (xf * rstd * gain).astype(jnp.bfloat16).reshape(rows, nlocal, BLOCK)
    left_p = pair_major(left_blocks)
    gate_p = pair_major(gate_blocks)
    act_a = jnp.einsum("tic,icj->tij", xn, left_p, preferred_element_type=jnp.float32)
    act_g = jnp.einsum("tic,icj->tij", xn, gate_p, preferred_element_type=jnp.float32)
    gated = (act_a * jax.nn.silu(act_g)).astype(jnp.bfloat16)
    outgoing = (
        gated.reshape(rows, nlocal, 2, NBLK).transpose(0, 3, 1, 2).reshape(rows, NBLK, 2 * nlocal)
    )
    returned = lax.all_to_all(grad_perm, "mp", split_axis=2, concat_axis=1, tiled=True)
    outgoing, xn_b = lax.optimization_barrier((outgoing, xn))
    me = lax.axis_index("mp")
    nmp = lax.axis_size("mp")
    width = outgoing.shape[1] // nmp
    arrived = [lax.dynamic_slice_in_dim(outgoing, me * width, width, axis=1)]
    for d in range(1, nmp):
        chunk = lax.dynamic_slice_in_dim(outgoing, (me ^ d) * width, width, axis=1)
        arrived.append(lax.ppermute(chunk, "mp", [(i, i ^ d) for i in range(nmp)]))
    act_a = jnp.einsum("tic,icj->tij", xn_b, left_p, preferred_element_type=jnp.float32)
    act_g = jnp.einsum("tic,icj->tij", xn_b, gate_p, preferred_element_type=jnp.float32)
    silu_g = jax.nn.silu(act_g)
    grad_gated = (
        returned.reshape(rows, NBLK, nlocal, 2)
        .transpose(0, 2, 3, 1)
        .reshape(rows, nlocal, BLOCK)
        .astype(jnp.float32)
    )
    sigma = jax.nn.sigmoid(act_g)
    grad_a = (grad_gated * silu_g).astype(jnp.bfloat16)
    grad_g = (grad_gated * act_a * sigma * (1.0 + act_g * (1.0 - sigma))).astype(jnp.bfloat16)
    left_local = pair_minor(jnp.einsum("tic,tij->icj", xn_b, grad_a, preferred_element_type=jnp.float32))
    gate_local = pair_minor(jnp.einsum("tic,tij->icj", xn_b, grad_g, preferred_element_type=jnp.float32))
    grad_norm = jnp.einsum("tij,icj->tic", grad_a, left_p, preferred_element_type=jnp.float32)
    grad_norm = grad_norm + jnp.einsum(
        "tij,icj->tic", grad_g, gate_p, preferred_element_type=jnp.float32
    )
    scaled = grad_norm.reshape(rows, width_local) * gain
    inner = lax.psum(jnp.sum(scaled * xf, axis=1), "mp")
    arrived, left_local, gate_local, scaled, inner = lax.optimization_barrier(
        (arrived, left_local, gate_local, scaled, inner)
    )
    permuted = jnp.stack(arrived, axis=2).reshape(rows, nlocal, BLOCK)
    by_partner = jnp.einsum(
        "tkc,tkm->kcm", permuted, cot_blocks, preferred_element_type=jnp.float32
    ).reshape(nlocal, nmp, BLOCK // nmp, BLOCK)
    right_local = jnp.concatenate(
        [lax.dynamic_index_in_dim(by_partner, me ^ b, axis=1, keepdims=False) for b in range(nmp)], axis=1
    )
    partials = (left_local, gate_local, right_local)
    mine = dp_reduce_scatter(partials)
    mean_inner = (inner / W)[:, None]
    grad_input = (
        cotangent.astype(jnp.float32) + rstd * (scaled - xf * rstd * rstd * mean_inner)
    ).astype(jnp.bfloat16)
    mine, grad_input = lax.optimization_barrier((mine, grad_input))
    left_total, gate_total, right_total = dp_all_gather(mine, [p.shape for p in partials])
    return (grad_input, left_total, gate_total, right_total)


def solution(mesh):
    placed = (
        P("dp", "mp"),
        P("mp"),
        P("mp", None, None),
        P("mp", None, None),
        P("mp", None, None),
        P("dp", "mp"),
    )
    return jax.shard_map(
        body,
        mesh=mesh,
        in_specs=placed,
        out_specs=(P("dp", "mp"), P("mp", None, None), P("mp", None, None), P("mp", None, None)),
        check_vma=False,
    )
```

```python
import jax
import jax.numpy as jnp
from jax import lax
from jax.sharding import PartitionSpec as P

W = 8192
BLOCK = 128
NBLK = 64


def dp_reduce_scatter(parts):
    ndp = lax.axis_size("dp")
    flat = jnp.concatenate([p.reshape(-1, BLOCK) for p in parts]).reshape(ndp, -1, BLOCK)
    got = lax.all_to_all(flat, "dp", 0, 0, tiled=True)
    return jnp.sum(got, axis=0)


def dp_all_gather(mine, shapes):
    ndp = lax.axis_size("dp")
    copies = jnp.broadcast_to(mine.astype(jnp.bfloat16)[None], (ndp,) + mine.shape)
    whole = lax.all_to_all(copies, "dp", 0, 0, tiled=True).reshape(-1, BLOCK, BLOCK)
    out, at = [], 0
    for shape in shapes:
        out.append(whole[at:at + shape[0]].astype(jnp.float32))
        at += shape[0]
    return tuple(out)


def mp_sum(v):
    n = lax.axis_size("mp")
    v = v + lax.ppermute(v, "mp", [(i, i ^ 1) for i in range(n)])
    return v + lax.ppermute(v, "mp", [(i, i ^ 2) for i in range(n)])


def pair_major(blocks):
    n, c, _ = blocks.shape
    return blocks.reshape(n, c, NBLK, 2).transpose(0, 1, 3, 2).reshape(n, c, 2 * NBLK)


def pair_minor(blocks):
    n, c, _ = blocks.shape
    return blocks.reshape(n, c, 2, NBLK).transpose(0, 1, 3, 2).reshape(n, c, 2 * NBLK)


def body(samples, gain, left_blocks, gate_blocks, right_blocks, cotangent):
    rows, width_local = samples.shape
    nlocal = left_blocks.shape[0]
    xf = samples.astype(jnp.float32)
    cot_blocks = cotangent.reshape(rows, nlocal, BLOCK)
    grad_perm = jnp.einsum(
        "tkm,kcm->tkc", cot_blocks, right_blocks, preferred_element_type=jnp.float32
    ).astype(jnp.bfloat16)
    squares = mp_sum(jnp.sum(xf * xf, axis=1))
    grad_perm, squares = lax.optimization_barrier((grad_perm, squares))
    rstd = lax.rsqrt(squares / W + 1e-05)[:, None]
    xn = (xf * rstd * gain).astype(jnp.bfloat16).reshape(rows, nlocal, BLOCK)
    left_p = pair_major(left_blocks)
    gate_p = pair_major(gate_blocks)
    act_a = jnp.einsum("tic,icj->tij", xn, left_p, preferred_element_type=jnp.float32)
    act_g = jnp.einsum("tic,icj->tij", xn, gate_p, preferred_element_type=jnp.float32)
    gated = (act_a * jax.nn.silu(act_g)).astype(jnp.bfloat16)
    outgoing = (
        gated.reshape(rows, nlocal, 2, NBLK).transpose(0, 3, 1, 2).reshape(rows, NBLK, 2 * nlocal)
    )
    returned = lax.all_to_all(grad_perm, "mp", split_axis=2, concat_axis=1, tiled=True)
    outgoing, xn_b = lax.optimization_barrier((outgoing, xn))
    me = lax.axis_index("mp")
    nmp = lax.axis_size("mp")
    width = outgoing.shape[1] // nmp
    arrived = [lax.dynamic_slice_in_dim(outgoing, me * width, width, axis=1)]
    for d in range(1, nmp):
        chunk = lax.dynamic_slice_in_dim(outgoing, (me ^ d) * width, width, axis=1)
        arrived.append(lax.ppermute(chunk, "mp", [(i, i ^ d) for i in range(nmp)]))
    act_a = jnp.einsum("tic,icj->tij", xn_b, left_p, preferred_element_type=jnp.float32)
    act_g = jnp.einsum("tic,icj->tij", xn_b, gate_p, preferred_element_type=jnp.float32)
    silu_g = jax.nn.silu(act_g)
    grad_gated = (
        returned.reshape(rows, NBLK, nlocal, 2)
        .transpose(0, 2, 3, 1)
        .reshape(rows, nlocal, BLOCK)
        .astype(jnp.float32)
    )
    sigma = jax.nn.sigmoid(act_g)
    grad_a = (grad_gated * silu_g).astype(jnp.bfloat16)
    grad_g = (grad_gated * act_a * sigma * (1.0 + act_g * (1.0 - sigma))).astype(jnp.bfloat16)
    left_local = pair_minor(jnp.einsum("tic,tij->icj", xn_b, grad_a, preferred_element_type=jnp.float32))
    gate_local = pair_minor(jnp.einsum("tic,tij->icj", xn_b, grad_g, preferred_element_type=jnp.float32))
    grad_norm = jnp.einsum("tij,icj->tic", grad_a, left_p, preferred_element_type=jnp.float32)
    grad_norm = grad_norm + jnp.einsum(
        "tij,icj->tic", grad_g, gate_p, preferred_element_type=jnp.float32
    )
    arrived, left_local, gate_local, grad_norm = lax.optimization_barrier(
        (arrived, left_local, gate_local, grad_norm)
    )
    permuted = jnp.stack(arrived, axis=2).reshape(rows, nlocal, BLOCK)
    by_partner = jnp.einsum(
        "tkc,tkm->kcm", permuted, cot_blocks, preferred_element_type=jnp.float32
    ).reshape(nlocal, nmp, BLOCK // nmp, BLOCK)
    right_local = jnp.concatenate(
        [lax.dynamic_index_in_dim(by_partner, me ^ b, axis=1, keepdims=False) for b in range(nmp)], axis=1
    )
    partials = (left_local, gate_local, right_local)
    mine = dp_reduce_scatter(partials)
    scaled = grad_norm.reshape(rows, width_local) * gain
    inner = lax.psum(jnp.sum(scaled * xf, axis=1), "mp")
    mean_inner = (inner / W)[:, None]
    grad_input = (
        cotangent.astype(jnp.float32) + rstd * (scaled - xf * rstd * rstd * mean_inner)
    ).astype(jnp.bfloat16)
    mine, grad_input = lax.optimization_barrier((mine, grad_input))
    left_total, gate_total, right_total = dp_all_gather(mine, [p.shape for p in partials])
    return (grad_input, left_total, gate_total, right_total)


def solution(mesh):
    placed = (
        P("dp", "mp"),
        P("mp"),
        P("mp", None, None),
        P("mp", None, None),
        P("mp", None, None),
        P("dp", "mp"),
    )
    return jax.shard_map(
        body,
        mesh=mesh,
        in_specs=placed,
        out_specs=(P("dp", "mp"), P("mp", None, None), P("mp", None, None), P("mp", None, None)),
        check_vma=False,
    )
```

```python
import jax
import jax.numpy as jnp
from jax import lax
from jax.sharding import PartitionSpec as P

W = 8192
BLOCK = 128
NBLK = 64


def dp_reduce_scatter(parts):
    ndp = lax.axis_size("dp")
    flat = jnp.concatenate([p.reshape(-1, BLOCK) for p in parts]).reshape(ndp, -1, BLOCK)
    got = lax.all_to_all(flat, "dp", 0, 0, tiled=True)
    return jnp.sum(got, axis=0)


def dp_all_gather(mine, shapes):
    ndp = lax.axis_size("dp")
    copies = jnp.broadcast_to(mine.astype(jnp.bfloat16)[None], (ndp,) + mine.shape)
    whole = lax.all_to_all(copies, "dp", 0, 0, tiled=True).reshape(-1, BLOCK, BLOCK)
    out, at = [], 0
    for shape in shapes:
        out.append(whole[at:at + shape[0]].astype(jnp.float32))
        at += shape[0]
    return tuple(out)


def mp_sum(v):
    n = lax.axis_size("mp")
    v = v + lax.ppermute(v, "mp", [(i, i ^ 1) for i in range(n)])
    return v + lax.ppermute(v, "mp", [(i, i ^ 2) for i in range(n)])


def pair_major(blocks):
    n, c, _ = blocks.shape
    return blocks.reshape(n, c, NBLK, 2).transpose(0, 1, 3, 2).reshape(n, c, 2 * NBLK)


def pair_minor(blocks):
    n, c, _ = blocks.shape
    return blocks.reshape(n, c, 2, NBLK).transpose(0, 1, 3, 2).reshape(n, c, 2 * NBLK)


def body(samples, gain, left_blocks, gate_blocks, right_blocks, cotangent):
    rows, width_local = samples.shape
    nlocal = left_blocks.shape[0]
    xf = samples.astype(jnp.float32)
    cot_blocks = cotangent.reshape(rows, nlocal, BLOCK)
    grad_perm = jnp.einsum(
        "tkm,kcm->tkc", cot_blocks, right_blocks, preferred_element_type=jnp.float32
    ).astype(jnp.bfloat16)
    squares = mp_sum(jnp.sum(xf * xf, axis=1))
    grad_perm, squares = lax.optimization_barrier((grad_perm, squares))
    rstd = lax.rsqrt(squares / W + 1e-05)[:, None]
    xn = (xf * rstd * gain).astype(jnp.bfloat16).reshape(rows, nlocal, BLOCK)
    left_p = pair_major(left_blocks)
    gate_p = pair_major(gate_blocks)
    act_a = jnp.einsum("tic,icj->tij", xn, left_p, preferred_element_type=jnp.float32)
    act_g = jnp.einsum("tic,icj->tij", xn, gate_p, preferred_element_type=jnp.float32)
    gated = (act_a * jax.nn.silu(act_g)).astype(jnp.bfloat16)
    outgoing = (
        gated.reshape(rows, nlocal, 2, NBLK).transpose(0, 3, 1, 2).reshape(rows, NBLK, 2 * nlocal)
    )
    returned = lax.all_to_all(grad_perm, "mp", split_axis=2, concat_axis=1, tiled=True)
    outgoing, xn_b = lax.optimization_barrier((outgoing, xn))
    me = lax.axis_index("mp")
    nmp = lax.axis_size("mp")
    width = outgoing.shape[1] // nmp
    arrived = [lax.dynamic_slice_in_dim(outgoing, me * width, width, axis=1)]
    for d in range(1, nmp):
        chunk = lax.dynamic_slice_in_dim(outgoing, (me ^ d) * width, width, axis=1)
        arrived.append(lax.ppermute(chunk, "mp", [(i, i ^ d) for i in range(nmp)]))
    act_a = jnp.einsum("tic,icj->tij", xn_b, left_p, preferred_element_type=jnp.float32)
    act_g = jnp.einsum("tic,icj->tij", xn_b, gate_p, preferred_element_type=jnp.float32)
    silu_g = jax.nn.silu(act_g)
    grad_gated = (
        returned.reshape(rows, NBLK, nlocal, 2)
        .transpose(0, 2, 3, 1)
        .reshape(rows, nlocal, BLOCK)
        .astype(jnp.float32)
    )
    sigma = jax.nn.sigmoid(act_g)
    grad_a = (grad_gated * silu_g).astype(jnp.bfloat16)
    grad_g = (grad_gated * act_a * sigma * (1.0 + act_g * (1.0 - sigma))).astype(jnp.bfloat16)
    left_local = pair_minor(jnp.einsum("tic,tij->icj", xn_b, grad_a, preferred_element_type=jnp.float32))
    gate_local = pair_minor(jnp.einsum("tic,tij->icj", xn_b, grad_g, preferred_element_type=jnp.float32))
    grad_norm = jnp.einsum("tij,icj->tic", grad_a, left_p, preferred_element_type=jnp.float32)
    grad_norm = grad_norm + jnp.einsum(
        "tij,icj->tic", grad_g, gate_p, preferred_element_type=jnp.float32
    )
    arrived, left_local, gate_local, grad_norm = lax.optimization_barrier(
        (arrived, left_local, gate_local, grad_norm)
    )
    permuted = jnp.stack(arrived, axis=2).reshape(rows, nlocal, BLOCK)
    by_partner = jnp.einsum(
        "tkc,tkm->kcm", permuted, cot_blocks, preferred_element_type=jnp.float32
    ).reshape(nlocal, nmp, BLOCK // nmp, BLOCK)
    right_local = jnp.concatenate(
        [lax.dynamic_index_in_dim(by_partner, me ^ b, axis=1, keepdims=False) for b in range(nmp)], axis=1
    )
    partials = (left_local, gate_local, right_local)
    mine = dp_reduce_scatter(partials)
    scaled = grad_norm.reshape(rows, width_local) * gain
    inner = mp_sum(jnp.sum(scaled * xf, axis=1))
    mean_inner = (inner / W)[:, None]
    grad_input = (
        cotangent.astype(jnp.float32) + rstd * (scaled - xf * rstd * rstd * mean_inner)
    ).astype(jnp.bfloat16)
    mine, grad_input = lax.optimization_barrier((mine, grad_input))
    left_total, gate_total, right_total = dp_all_gather(mine, [p.shape for p in partials])
    return (grad_input, left_total, gate_total, right_total)


def solution(mesh):
    placed = (
        P("dp", "mp"),
        P("mp"),
        P("mp", None, None),
        P("mp", None, None),
        P("mp", None, None),
        P("dp", "mp"),
    )
    return jax.shard_map(
        body,
        mesh=mesh,
        in_specs=placed,
        out_specs=(P("dp", "mp"), P("mp", None, None), P("mp", None, None), P("mp", None, None)),
        check_vma=False,
    )
```

```python
import jax
import jax.numpy as jnp
from jax import lax
from jax.sharding import PartitionSpec as P

W = 8192
BLOCK = 128
NBLK = 64


def dp_reduce_scatter(parts):
    ndp = lax.axis_size("dp")
    flat = jnp.concatenate([p.reshape(-1, BLOCK) for p in parts]).reshape(ndp, -1, BLOCK)
    got = lax.all_to_all(flat, "dp", 0, 0, tiled=True)
    return jnp.sum(got, axis=0)


def dp_all_gather(mine, shapes):
    ndp = lax.axis_size("dp")
    copies = jnp.broadcast_to(mine.astype(jnp.bfloat16)[None], (ndp,) + mine.shape)
    whole = lax.all_to_all(copies, "dp", 0, 0, tiled=True).reshape(-1, BLOCK, BLOCK)
    out, at = [], 0
    for shape in shapes:
        out.append(whole[at:at + shape[0]].astype(jnp.float32))
        at += shape[0]
    return tuple(out)


def mp_sum(v):
    n = lax.axis_size("mp")
    v = v + lax.ppermute(v, "mp", [(i, i ^ 1) for i in range(n)])
    return v + lax.ppermute(v, "mp", [(i, i ^ 2) for i in range(n)])


def pair_major(blocks):
    n, c, _ = blocks.shape
    return blocks.reshape(n, c, NBLK, 2).transpose(0, 1, 3, 2).reshape(n, c, 2 * NBLK)


def pair_minor(blocks):
    n, c, _ = blocks.shape
    return blocks.reshape(n, c, 2, NBLK).transpose(0, 1, 3, 2).reshape(n, c, 2 * NBLK)


def body(samples, gain, left_blocks, gate_blocks, right_blocks, cotangent):
    rows, width_local = samples.shape
    nlocal = left_blocks.shape[0]
    xf = samples.astype(jnp.float32)
    cot_blocks = cotangent.reshape(rows, nlocal, BLOCK)
    grad_perm = jnp.einsum(
        "tkm,kcm->ckt", cot_blocks, right_blocks, preferred_element_type=jnp.float32
    ).astype(jnp.bfloat16)
    squares = mp_sum(jnp.sum(xf * xf, axis=1))
    grad_perm, squares = lax.optimization_barrier((grad_perm, squares))
    rstd = lax.rsqrt(squares / W + 1e-05)[:, None]
    xn = (xf * rstd * gain).astype(jnp.bfloat16).reshape(rows, nlocal, BLOCK)
    left_p = pair_major(left_blocks)
    gate_p = pair_major(gate_blocks)
    act_a = jnp.einsum("tic,icj->tij", xn, left_p, preferred_element_type=jnp.float32)
    act_g = jnp.einsum("tic,icj->tij", xn, gate_p, preferred_element_type=jnp.float32)
    gated = (act_a * jax.nn.silu(act_g)).astype(jnp.bfloat16)
    outgoing = (
        gated.reshape(rows, nlocal, 2, NBLK).transpose(0, 3, 1, 2).reshape(rows, NBLK, 2 * nlocal)
    )
    returned = lax.all_to_all(grad_perm, "mp", split_axis=0, concat_axis=1, tiled=True).transpose(2, 1, 0)
    outgoing, xn_b = lax.optimization_barrier((outgoing, xn))
    me = lax.axis_index("mp")
    nmp = lax.axis_size("mp")
    width = outgoing.shape[1] // nmp
    arrived = [lax.dynamic_slice_in_dim(outgoing, me * width, width, axis=1)]
    for d in range(1, nmp):
        chunk = lax.dynamic_slice_in_dim(outgoing, (me ^ d) * width, width, axis=1)
        arrived.append(lax.ppermute(chunk, "mp", [(i, i ^ d) for i in range(nmp)]))
    act_a = jnp.einsum("tic,icj->tij", xn_b, left_p, preferred_element_type=jnp.float32)
    act_g = jnp.einsum("tic,icj->tij", xn_b, gate_p, preferred_element_type=jnp.float32)
    silu_g = jax.nn.silu(act_g)
    grad_gated = (
        returned.reshape(rows, NBLK, nlocal, 2)
        .transpose(0, 2, 3, 1)
        .reshape(rows, nlocal, BLOCK)
        .astype(jnp.float32)
    )
    sigma = jax.nn.sigmoid(act_g)
    grad_a = (grad_gated * silu_g).astype(jnp.bfloat16)
    grad_g = (grad_gated * act_a * sigma * (1.0 + act_g * (1.0 - sigma))).astype(jnp.bfloat16)
    left_local = pair_minor(jnp.einsum("tic,tij->icj", xn_b, grad_a, preferred_element_type=jnp.float32))
    gate_local = pair_minor(jnp.einsum("tic,tij->icj", xn_b, grad_g, preferred_element_type=jnp.float32))
    grad_norm = jnp.einsum("tij,icj->tic", grad_a, left_p, preferred_element_type=jnp.float32)
    grad_norm = grad_norm + jnp.einsum(
        "tij,icj->tic", grad_g, gate_p, preferred_element_type=jnp.float32
    )
    arrived, left_local, gate_local, grad_norm = lax.optimization_barrier(
        (arrived, left_local, gate_local, grad_norm)
    )
    permuted = jnp.stack(arrived, axis=2).reshape(rows, nlocal, BLOCK)
    by_partner = jnp.einsum(
        "tkc,tkm->kcm", permuted, cot_blocks, preferred_element_type=jnp.float32
    ).reshape(nlocal, nmp, BLOCK // nmp, BLOCK)
    right_local = jnp.concatenate(
        [lax.dynamic_index_in_dim(by_partner, me ^ b, axis=1, keepdims=False) for b in range(nmp)], axis=1
    )
    partials = (left_local, gate_local, right_local)
    mine = dp_reduce_scatter(partials)
    scaled = grad_norm.reshape(rows, width_local) * gain
    inner = mp_sum(jnp.sum(scaled * xf, axis=1))
    mean_inner = (inner / W)[:, None]
    grad_input = (
        cotangent.astype(jnp.float32) + rstd * (scaled - xf * rstd * rstd * mean_inner)
    ).astype(jnp.bfloat16)
    mine, grad_input = lax.optimization_barrier((mine, grad_input))
    left_total, gate_total, right_total = dp_all_gather(mine, [p.shape for p in partials])
    return (grad_input, left_total, gate_total, right_total)


def solution(mesh):
    placed = (
        P("dp", "mp"),
        P("mp"),
        P("mp", None, None),
        P("mp", None, None),
        P("mp", None, None),
        P("dp", "mp"),
    )
    return jax.shard_map(
        body,
        mesh=mesh,
        in_specs=placed,
        out_specs=(P("dp", "mp"), P("mp", None, None), P("mp", None, None), P("mp", None, None)),
        check_vma=False,
    )
```
